512 devices in a mesh: dp: 64 (over x_lo, z, core), tensor: 8 (over x_hi, y).
Axes of the slice: x: 4 (x_hi: 2, x_lo: 2; x = x_hi * 2 + x_lo), y: 4, z: 16, core: 2. Of those that a mesh axis runs over, the one named last changes fastest.
Arguments:
- gate_act: bfloat16 [8192, 14336], P('dp', 'tensor'), may hold values from -6 to 6
- up_act: bfloat16 [8192, 14336], P('dp', 'tensor'), may hold values from -6 to 6
- d_out: bfloat16 [8192, 4096], P(('dp', 'tensor')), may hold values from -6 to 6
- w_tiles: bfloat16 [8, 18816, 128], P('tensor', 'dp'), may hold values from -0.09375 to 0.09375
- row_ptr: int32 [8, 5], P('tensor'), may hold values from 0 to 42, as said below
- col_idx: int32 [8, 42], P('tensor'), may hold values from 0 to 31, as said below
Outputs:
- out: bfloat16 [8192, 4096], P(('dp', 'tensor'))
- d_gate: bfloat16 [8192, 14336], P('dp', 'tensor')
- d_up: bfloat16 [8192, 14336], P('dp', 'tensor')
- d_weight: float32 [8, 18816, 128], P('tensor', 'dp')
The draws below stay inside these ranges and needn't reach their ends.
Inputs may be any that keep to these rules, and one draw needn't show every extreme that they name: row_ptr[t] starts at 0 and never falls; its last entry is shard t's count of nonzero tiles, at most 42, and some shard has exactly 42. For a live slot k of shard t, col_idx[t, k] is the block column of shard t's k-th nonzero tile in row-major order of the tile grid; a shard's tiles are distinct. Slots past the count hold 0.
All inputs are finite; a program needn't handle non-finite values.
Results may differ from the reference program's by a relative error of at most 0.015.
Values may be sent and summed in bfloat16 or wider, within the bound.
No kernel may reach another device: no remote copies, remote signals or barrier semaphores. Data moves between devices by JAX's collectives and lax.ppermute only.
A program may use at most 128 MiB of HBM per device.

```python
import jax
import jax.numpy as jnp
from jax import lax

D = 4096
FF = 14336
TF = 448
TD = 128
CAP = 42
TOKENS = 8192
N_TENSOR = 8


def tile_lists(key):
    base = jax.random.fold_in(key, 4242)
    row_blocks = FF // N_TENSOR // TF
    col_blocks = D // TD
    total_tiles = row_blocks * col_blocks
    lowest = CAP - CAP // 4
    count_key, pick_key, full_key = jax.random.split(base, 3)
    counts = jax.random.randint(count_key, (N_TENSOR,), lowest, CAP + 1)
    fullest = jax.random.randint(full_key, (), 0, N_TENSOR)
    counts = jnp.where(jnp.arange(N_TENSOR) == fullest, CAP, counts)
    shard_keys = jax.random.split(pick_key, N_TENSOR)

    def one_shard(shard_key, shard_count):
        order = jax.random.permutation(shard_key, total_tiles)[:CAP]
        slot_indices = jnp.arange(CAP)
        live = slot_indices < shard_count
        sorted_ids = jnp.sort(jnp.where(live, order, total_tiles + slot_indices))
        columns = jnp.where(live, sorted_ids % col_blocks, 0)
        bounds = jnp.arange(row_blocks + 1) * col_blocks
        pointers = jnp.sum(((sorted_ids[None, :] < bounds[:, None]) & live[None, :]).astype(jnp.int32), axis=1)
        return (pointers, columns)
    pointers, columns = jax.vmap(one_shard)(shard_keys, counts)
    return (pointers.astype(jnp.int32), columns.astype(jnp.int32))


def draw_row_ptr(key, part):
    return tile_lists(key)[0]


def draw_col_idx(key, part):
    return tile_lists(key)[1]


def steps_of(key, extent, cuts, smallest, high):
    factor_of, own = 1.0, jax.random.fold_in(key, 6)
    for dim, blocks in cuts:
        steps = jnp.exp(jax.random.uniform(jax.random.fold_in(own, dim), (blocks,), jnp.float32, smallest / len(cuts), high / len(cuts)))
        factor_of = factor_of * jnp.repeat(steps, extent[dim] // blocks).reshape([-1 if axis == dim else 1 for axis in range(len(extent))])
    return factor_of


def bell_draw(rng, extent, deviation, limit, cuts=(), kind=jnp.bfloat16):
    drawn = deviation * jax.random.normal(rng, extent, jnp.float32)
    if cuts:
        drawn = drawn * steps_of(rng, extent, cuts, -0.22, 0.18)
    return jnp.clip(drawn, -limit, limit).astype(kind)


def setup_inputs(seed: int = 0) -> dict:
    splits = jax.random.split(jax.random.key(seed), 7)
    return {
        "gate_act": bell_draw(splits[0], (TOKENS, FF), 1.0, 6.0, ((0, 64), (1, 8))),
        "up_act": bell_draw(splits[1], (TOKENS, FF), 1.0, 6.0, ((0, 64), (1, 8))),
        "d_out": bell_draw(splits[2], (TOKENS, D), 1.0, 6.0, ((0, 512),)),
        "w_tiles": bell_draw(splits[3], (N_TENSOR, CAP * TF, TD), (FF * 3 // 10) ** -0.5, 0.09375, ((0, 8), (1, 64))),
        "row_ptr": draw_row_ptr(jax.random.fold_in(splits[6], 71), 0),
        "col_idx": draw_col_idx(jax.random.fold_in(splits[6], 71), 0),
    }


def slot_layout(row_ptr, col_idx):
    slot_indices = jnp.arange(CAP, dtype=jnp.int32)
    tile_rows = jnp.sum((row_ptr[:, 1:, None] <= slot_indices[None, None, :]).astype(jnp.int32), axis=1)
    live = slot_indices[None, :] < row_ptr[:, -1:]
    tile_rows = jnp.where(live, tile_rows, 0).astype(jnp.int32)
    tile_cols = jnp.where(live, col_idx, 0).astype(jnp.int32)
    return tile_rows, tile_cols, live


def dense_weight(w_tiles, tile_rows, tile_cols, live):
    row_blocks = FF // N_TENSOR // TF
    col_blocks = D // TD
    pieces = w_tiles.reshape(N_TENSOR, CAP, TF, TD).astype(jnp.float32) * live[:, :, None, None].astype(jnp.float32)
    shard_ids = jnp.broadcast_to(jnp.arange(N_TENSOR, dtype=jnp.int32)[:, None], (N_TENSOR, CAP))
    dense = jnp.zeros((N_TENSOR, row_blocks, col_blocks, TF, TD), jnp.float32)
    dense = dense.at[shard_ids, tile_rows, tile_cols].add(pieces)
    dense = dense.transpose(0, 1, 3, 2, 4).reshape(N_TENSOR, FF // N_TENSOR, D)
    return dense.astype(jnp.bfloat16)


def reference(gate_act, up_act, d_out, w_tiles, row_ptr, col_idx):
    tile_rows, tile_cols, live = slot_layout(row_ptr, col_idx)
    weight = dense_weight(w_tiles, tile_rows, tile_cols, live)
    width_shard = FF // N_TENSOR
    gate = gate_act.astype(jnp.float32)
    upper = up_act.astype(jnp.float32)
    sigmoid_gate = jax.nn.sigmoid(gate)
    hidden = (gate * sigmoid_gate * upper).astype(jnp.bfloat16)
    hidden_shards = hidden.reshape(TOKENS, N_TENSOR, width_shard).transpose(1, 0, 2)

    def add_shard(total, pair):
        part = jnp.dot(pair[0], pair[1], preferred_element_type=jnp.float32).astype(jnp.bfloat16)
        part = lax.optimization_barrier(part)
        return total + part.astype(jnp.float32), None

    total, _ = lax.scan(add_shard, jnp.zeros((TOKENS, D), jnp.float32), (hidden_shards, weight))
    out = total.astype(jnp.bfloat16)

    def shard_back(shard_weight):
        return jnp.dot(d_out, shard_weight.T, preferred_element_type=jnp.float32)

    d_hidden = lax.map(shard_back, weight).transpose(1, 0, 2).reshape(TOKENS, FF)
    d_up = (d_hidden * gate * sigmoid_gate).astype(jnp.bfloat16)
    d_gate = (d_hidden * upper * sigmoid_gate * (1.0 + gate * (1.0 - sigmoid_gate))).astype(jnp.bfloat16)

    row_blocks = width_shard // TF
    col_blocks = D // TD

    def shard_gradient(items):
        shard_hidden, rows_here, cols_here, live_here = items
        full = jnp.dot(shard_hidden.T, d_out, preferred_element_type=jnp.float32)
        full = full.reshape(row_blocks, TF, col_blocks, TD)
        picked = full[rows_here, :, cols_here, :]
        return picked * live_here.astype(jnp.float32)[:, None, None]

    tile_grads = lax.map(shard_gradient, (hidden_shards, tile_rows, tile_cols, live))
    d_weight = tile_grads.reshape(N_TENSOR, CAP * TF, TD)
    return out, d_gate, d_up, d_weight
```

```python
import jax
import jax.numpy as jnp
from jax import lax
from jax.sharding import PartitionSpec as P

TF = 448
TD = 128
CAP = 42

DP_BITS_CHEAP_FIRST = (0, 5, 1, 2, 3, 4)


def _bit_order(n):
    bits = [b for b in DP_BITS_CHEAP_FIRST if (1 << b) < n]
    assert (1 << len(bits)) == n
    return bits


def _swap(x, axis, bit, n):
    perm = [(i, i ^ (1 << bit)) for i in range(n)]
    return lax.ppermute(x, axis, perm)


def tree_all_gather(block, axis):
    n = lax.axis_size(axis)
    me = lax.axis_index(axis)
    bits = _bit_order(n)[::-1]
    acc = block
    for bit in bits:
        other = _swap(acc, axis, bit, n)
        high = ((me >> bit) & 1) == 1
        lo = jnp.where(high, other, acc)
        hi = jnp.where(high, acc, other)
        acc = jnp.stack([lo, hi])
    k = len(bits)
    held = bits[::-1]
    order = sorted(range(k), key=lambda a: -held[a])
    acc = jnp.transpose(acc, tuple(order) + tuple(range(k, k + block.ndim)))
    return acc.reshape((n * block.shape[0],) + block.shape[1:])


def tree_reduce_scatter(full, axis, wire_dtype):
    n = lax.axis_size(axis)
    me = lax.axis_index(axis)
    bits = _bit_order(n)
    k = len(bits)
    rows = full.shape[0] // n
    acc = full.astype(jnp.float32).reshape((2,) * k + (rows,) + full.shape[1:])
    present = list(range(k - 1, -1, -1))
    for bit in bits:
        a = present.index(bit)
        high = ((me >> bit) & 1) == 1
        zero = lax.index_in_dim(acc, 0, a, keepdims=False)
        one = lax.index_in_dim(acc, 1, a, keepdims=False)
        keep = jnp.where(high, one, zero)
        send = jnp.where(high, zero, one)
        got = _swap(send.astype(wire_dtype), axis, bit, n)
        acc = keep + got.astype(jnp.float32)
        present.pop(a)
    return acc


def slot_layout(row_ptr, col_idx):
    slots = jnp.arange(CAP, dtype=jnp.int32)
    tile_rows = jnp.sum((row_ptr[0, 1:, None] <= slots[None, :]).astype(jnp.int32), axis=0)
    live = slots < row_ptr[0, -1]
    tile_rows = jnp.where(live, tile_rows, 0)
    tile_cols = jnp.where(live, col_idx[0], 0)
    return tile_rows, tile_cols, live


def on_device(gate_act, up_act, d_out, w_tiles, row_ptr, col_idx):
    group_rows, width_shard = gate_act.shape
    width = d_out.shape[1]
    row_blocks = width_shard // TF
    col_blocks = width // TD
    tile_rows, tile_cols, live = slot_layout(row_ptr, col_idx)

    gate = gate_act.astype(jnp.float32)
    upper = up_act.astype(jnp.float32)
    sigmoid_gate = jax.nn.sigmoid(gate)
    silu = gate * sigmoid_gate
    hidden = (silu * upper).astype(jnp.bfloat16)

    d_group = lax.all_gather(d_out, "tensor", axis=0, tiled=True)
    hidden_rows = hidden.reshape(group_rows, row_blocks, TF)[:, tile_rows, :]
    d_cols = d_group.reshape(group_rows, col_blocks, TD)[:, tile_cols, :]
    tile_grad = jnp.einsum("tkf,tkd->kfd", hidden_rows, d_cols, preferred_element_type=jnp.float32)
    tile_grad = tile_grad * live[:, None, None].astype(jnp.float32)
    d_weight = tree_reduce_scatter(tile_grad.reshape(CAP * TF, TD), "dp", jnp.bfloat16)

    gathered = tree_all_gather(w_tiles[0], "dp").reshape(CAP, TF, TD)
    tiles = jnp.where(live[:, None, None], gathered, jnp.zeros_like(gathered))
    place_rows = jnp.where(live, tile_rows, row_blocks)
    dense = jnp.zeros((row_blocks, col_blocks, TF, TD), jnp.bfloat16)
    dense = dense.at[place_rows, tile_cols].set(tiles, mode="drop")

    partial = jnp.einsum(
        "trf,rcfd->tcd",
        hidden.reshape(group_rows, row_blocks, TF),
        dense,
        preferred_element_type=jnp.float32,
    ).astype(jnp.bfloat16)
    out = lax.psum_scatter(
        partial.reshape(group_rows, width), "tensor", scatter_dimension=0, tiled=True
    )

    d_hidden = jnp.einsum(
        "tcd,rcfd->trf",
        d_group.reshape(group_rows, col_blocks, TD),
        dense,
        preferred_element_type=jnp.float32,
    ).reshape(group_rows, width_shard)
    d_up = (d_hidden * silu).astype(jnp.bfloat16)
    d_gate = (d_hidden * upper * sigmoid_gate * (1.0 + gate * (1.0 - sigmoid_gate))).astype(
        jnp.bfloat16
    )
    return (out, d_gate, d_up, d_weight[None])


def solution(mesh):
    return jax.shard_map(
        on_device,
        mesh=mesh,
        in_specs=(
            P("dp", "tensor"),
            P("dp", "tensor"),
            P(("dp", "tensor"), None),
            P("tensor", "dp", None),
            P("tensor", None),
            P("tensor", None),
        ),
        out_specs=(
            P(("dp", "tensor"), None),
            P("dp", "tensor"),
            P("dp", "tensor"),
            P("tensor", "dp", None),
        ),
        check_vma=False,
    )
```

```python
import jax
import jax.numpy as jnp
from jax import lax
from jax.sharding import PartitionSpec as P

TF = 448
TD = 128
CAP = 42

DP_BITS_CHEAP_FIRST = (0, 5, 1, 2, 3, 4)


def _bit_order(n):
    bits = [b for b in DP_BITS_CHEAP_FIRST if (1 << b) < n]
    assert (1 << len(bits)) == n
    return bits


def _swap(x, axis, bit, n):
    perm = [(i, i ^ (1 << bit)) for i in range(n)]
    return lax.ppermute(x, axis, perm)


def tree_all_gather(block, axis):
    n = lax.axis_size(axis)
    me = lax.axis_index(axis)
    bits = _bit_order(n)[::-1]
    acc = block
    for bit in bits:
        other = _swap(acc, axis, bit, n)
        high = ((me >> bit) & 1) == 1
        lo = jnp.where(high, other, acc)
        hi = jnp.where(high, acc, other)
        acc = jnp.stack([lo, hi])
    k = len(bits)
    held = bits[::-1]
    order = sorted(range(k), key=lambda a: -held[a])
    acc = jnp.transpose(acc, tuple(order) + tuple(range(k, k + block.ndim)))
    return acc.reshape((n * block.shape[0],) + block.shape[1:])


def tree_reduce_scatter(full, axis, wire_dtype):
    n = lax.axis_size(axis)
    me = lax.axis_index(axis)
    bits = _bit_order(n)
    k = len(bits)
    rows = full.shape[0] // n
    acc = full.astype(jnp.float32).reshape((2,) * k + (rows,) + full.shape[1:])
    present = list(range(k - 1, -1, -1))
    for bit in bits:
        a = present.index(bit)
        high = ((me >> bit) & 1) == 1
        zero = lax.index_in_dim(acc, 0, a, keepdims=False)
        one = lax.index_in_dim(acc, 1, a, keepdims=False)
        keep = jnp.where(high, one, zero)
        send = jnp.where(high, zero, one)
        got = _swap(send.astype(wire_dtype), axis, bit, n)
        acc = keep + got.astype(jnp.float32)
        present.pop(a)
    return acc


def slot_layout(row_ptr, col_idx):
    slots = jnp.arange(CAP, dtype=jnp.int32)
    tile_rows = jnp.sum((row_ptr[0, 1:, None] <= slots[None, :]).astype(jnp.int32), axis=0)
    live = slots < row_ptr[0, -1]
    tile_rows = jnp.where(live, tile_rows, 0)
    tile_cols = jnp.where(live, col_idx[0], 0)
    return tile_rows, tile_cols, live


def on_device(gate_act, up_act, d_out, w_tiles, row_ptr, col_idx):
    group_rows, width_shard = gate_act.shape
    width = d_out.shape[1]
    row_blocks = width_shard // TF
    col_blocks = width // TD
    tile_rows, tile_cols, live = slot_layout(row_ptr, col_idx)

    d_group = lax.all_gather(d_out, "tensor", axis=0, tiled=True)

    gate = gate_act.astype(jnp.float32)
    upper = up_act.astype(jnp.float32)
    sigmoid_gate = jax.nn.sigmoid(gate)
    silu = gate * sigmoid_gate
    hidden = (silu * upper).astype(jnp.bfloat16)

    hidden_rows = hidden.reshape(group_rows, row_blocks, TF).transpose(1, 0, 2)[tile_rows]
    d_cols = d_group.reshape(group_rows, col_blocks, TD).transpose(1, 0, 2)[tile_cols]

    tile_grad = jnp.einsum("ktf,ktd->kfd", hidden_rows, d_cols, preferred_element_type=jnp.float32)
    tile_grad = jnp.where(live[:, None, None], tile_grad, jnp.zeros_like(tile_grad))
    w_block, tile_grad = lax.optimization_barrier((w_tiles[0], tile_grad))
    gathered = lax.all_gather(w_block, "dp", axis=0, tiled=True).reshape(CAP, TF, TD)
    owners = lax.axis_size("dp")
    d_weight = lax.psum_scatter(
        tile_grad.reshape(owners, CAP * TF // owners, TD), "dp", scatter_dimension=0, tiled=True
    )

    tiles = jnp.where(live[:, None, None], gathered, jnp.zeros_like(gathered))
    col_place = (tile_cols[:, None] == jnp.arange(col_blocks, dtype=jnp.int32)[None, :]) & live[:, None]
    row_place = (tile_rows[:, None] == jnp.arange(row_blocks, dtype=jnp.int32)[None, :]) & live[:, None]

    products = jnp.einsum("ktf,kfd->ktd", hidden_rows, tiles, preferred_element_type=jnp.float32)
    partial = jnp.einsum(
        "ktd,kc->tcd", products, col_place.astype(jnp.float32), precision=lax.Precision.HIGHEST
    ).astype(jnp.bfloat16)
    out = lax.psum_scatter(
        partial.reshape(group_rows, width), "tensor", scatter_dimension=0, tiled=True
    )

    back = jnp.einsum("ktd,kfd->ktf", d_cols, tiles, preferred_element_type=jnp.float32)
    d_hidden = jnp.einsum(
        "ktf,kr->trf", back, row_place.astype(jnp.float32), precision=lax.Precision.HIGHEST
    ).reshape(group_rows, width_shard)
    d_up = (d_hidden * silu).astype(jnp.bfloat16)
    d_gate = (d_hidden * upper * sigmoid_gate * (1.0 + gate * (1.0 - sigmoid_gate))).astype(
        jnp.bfloat16
    )
    return (out, d_gate, d_up, d_weight)


def solution(mesh):
    return jax.shard_map(
        on_device,
        mesh=mesh,
        in_specs=(
            P("dp", "tensor"),
            P("dp", "tensor"),
            P(("dp", "tensor"), None),
            P("tensor", "dp", None),
            P("tensor", None),
            P("tensor", None),
        ),
        out_specs=(
            P(("dp", "tensor"), None),
            P("dp", "tensor"),
            P("dp", "tensor"),
            P("tensor", "dp", None),
        ),
        check_vma=False,
    )
```

```python
import jax
import jax.numpy as jnp
from jax import lax
from jax.sharding import PartitionSpec as P

TF = 448
TD = 128
CAP = 42

BITS_CHEAP_FIRST = {"dp": (0, 5, 1, 2, 3, 4), "tensor": (0, 1, 2)}


def _bit_order(axis, n):
    bits = [b for b in BITS_CHEAP_FIRST[axis] if (1 << b) < n]
    bits += [b for b in range(n.bit_length() - 1) if b not in bits]
    assert (1 << len(bits)) == n
    return bits


def _swap(x, axis, bit, n):
    perm = [(i, i ^ (1 << bit)) for i in range(n)]
    return lax.ppermute(x, axis, perm)


def tree_all_gather(block, axis):
    n = lax.axis_size(axis)
    me = lax.axis_index(axis)
    bits = _bit_order(axis, n)[::-1]
    acc = block
    for bit in bits:
        other = _swap(acc, axis, bit, n)
        high = ((me >> bit) & 1) == 1
        lo = jnp.where(high, other, acc)
        hi = jnp.where(high, acc, other)
        acc = jnp.stack([lo, hi])
    k = len(bits)
    held = bits[::-1]
    order = sorted(range(k), key=lambda a: -held[a])
    acc = jnp.transpose(acc, tuple(order) + tuple(range(k, k + block.ndim)))
    return acc.reshape((n * block.shape[0],) + block.shape[1:])


def tree_reduce_scatter(full, axis, wire_dtypes):
    n = lax.axis_size(axis)
    me = lax.axis_index(axis)
    bits = _bit_order(axis, n)
    k = len(bits)
    rows = full.shape[0] // n
    acc = full.astype(jnp.float32).reshape((2,) * k + (rows,) + full.shape[1:])
    present = list(range(k - 1, -1, -1))
    for stage, bit in enumerate(bits):
        a = present.index(bit)
        high = ((me >> bit) & 1) == 1
        zero = lax.index_in_dim(acc, 0, a, keepdims=False)
        one = lax.index_in_dim(acc, 1, a, keepdims=False)
        keep = jnp.where(high, one, zero)
        send = jnp.where(high, zero, one)
        got = _swap(send.astype(wire_dtypes[stage]), axis, bit, n)
        acc = keep + got.astype(jnp.float32)
        present.pop(a)
    return acc


def slot_layout(row_ptr, col_idx):
    slots = jnp.arange(CAP, dtype=jnp.int32)
    tile_rows = jnp.sum((row_ptr[0, 1:, None] <= slots[None, :]).astype(jnp.int32), axis=0)
    live = slots < row_ptr[0, -1]
    tile_rows = jnp.where(live, tile_rows, 0)
    tile_cols = jnp.where(live, col_idx[0], 0)
    return tile_rows, tile_cols, live


def on_device(gate_act, up_act, d_out, w_tiles, row_ptr, col_idx):
    group_rows, width_shard = gate_act.shape
    width = d_out.shape[1]
    row_blocks = width_shard // TF
    col_blocks = width // TD
    tile_rows, tile_cols, live = slot_layout(row_ptr, col_idx)

    gathered = tree_all_gather(w_tiles[0], "dp").reshape(CAP, TF, TD)
    d_group = tree_all_gather(d_out, "tensor")

    gate = gate_act.astype(jnp.float32)
    upper = up_act.astype(jnp.float32)
    sigmoid_gate = jax.nn.sigmoid(gate)
    silu = gate * sigmoid_gate
    hidden = (silu * upper).astype(jnp.bfloat16)

    hidden_rows = hidden.reshape(group_rows, row_blocks, TF).transpose(1, 0, 2)[tile_rows]
    d_cols = d_group.reshape(group_rows, col_blocks, TD).transpose(1, 0, 2)[tile_cols]

    tile_grad = jnp.einsum("ktf,ktd->kfd", hidden_rows, d_cols, preferred_element_type=jnp.float32)
    tile_grad = jnp.where(live[:, None, None], tile_grad, jnp.zeros_like(tile_grad))
    d_weight = tree_reduce_scatter(tile_grad.reshape(CAP * TF, TD), "dp", (jnp.bfloat16,) * 6)

    tiles = jnp.where(live[:, None, None], gathered, jnp.zeros_like(gathered))
    col_place = (tile_cols[:, None] == jnp.arange(col_blocks, dtype=jnp.int32)[None, :]) & live[:, None]
    row_place = (tile_rows[:, None] == jnp.arange(row_blocks, dtype=jnp.int32)[None, :]) & live[:, None]

    products = jnp.einsum("ktf,kfd->ktd", hidden_rows, tiles, preferred_element_type=jnp.float32)
    partial = jnp.einsum(
        "ktd,kc->tcd", products, col_place.astype(jnp.float32), precision=lax.Precision.HIGHEST
    ).astype(jnp.bfloat16)
    out = tree_reduce_scatter(
        partial.reshape(group_rows, width), "tensor", (jnp.bfloat16,) + (jnp.float32,) * 2
    ).astype(jnp.bfloat16)

    back = jnp.einsum("ktd,kfd->ktf", d_cols, tiles, preferred_element_type=jnp.float32)
    d_hidden = jnp.einsum(
        "ktf,kr->trf", back, row_place.astype(jnp.float32), precision=lax.Precision.HIGHEST
    ).reshape(group_rows, width_shard)
    d_up = (d_hidden * silu).astype(jnp.bfloat16)
    d_gate = (d_hidden * upper * sigmoid_gate * (1.0 + gate * (1.0 - sigmoid_gate))).astype(
        jnp.bfloat16
    )
    return (out, d_gate, d_up, d_weight[None])


def solution(mesh):
    return jax.shard_map(
        on_device,
        mesh=mesh,
        in_specs=(
            P("dp", "tensor"),
            P("dp", "tensor"),
            P(("dp", "tensor"), None),
            P("tensor", "dp", None),
            P("tensor", None),
            P("tensor", None),
        ),
        out_specs=(
            P(("dp", "tensor"), None),
            P("dp", "tensor"),
            P("dp", "tensor"),
            P("tensor", "dp", None),
        ),
        check_vma=False,
    )
```
